512 devices in a mesh: chan: 32 (over x_lo, z), freq: 16 (over y, x_hi, core).
Axes of the slice: x: 4 (x_hi: 2, x_lo: 2; x = x_hi * 2 + x_lo), y: 4, z: 16, core: 2. Of those that a mesh axis runs over, the one named last changes fastest.
Arguments:
- traces: bfloat16 [4096, 81920], P('chan', 'freq'), may hold values from -2000 to 2000
- kept_bins: int32 [128], replicated, may hold values from 1 to 255, as said below
- round_masks: int32 [2], replicated, may hold values from 1 to 31, as said below
Outputs:
- cross_spectra: float32 [2, 128, 2, 4096, 128], P(None, 'freq', None, 'chan')
- auto_spectra: float32 [128, 2, 4096, 128], P('freq', None, 'chan')
The draws below stay inside these ranges and needn't reach their ends.
Inputs may be any that keep to these rules, and one draw needn't show every extreme that they name: `kept_bins`: 128 distinct bin numbers in increasing order; 1 and 255 are among them. `round_masks`: 2 distinct numbers; in round r channel block b is paired with block b XOR round_masks[r].
All inputs are finite; a program needn't handle non-finite values.
Results may differ from the reference program's by a relative error of at most 0.0066.
Values may be sent and summed in bfloat16 or wider, within the bound.
No kernel may reach another device: no remote copies, remote signals or barrier semaphores. Data moves between devices by JAX's collectives and lax.ppermute only.
A program may use at most 64 MiB of HBM per device.

```python
import math
import jax
import jax.numpy as jnp
from jax import lax

NS = 512
HOP = 256
KEEP = 128
CH = 128
ROUNDS = 2
WINDOWS = 320
SAMPLES = 81920
CHANNELS = 4096
N_CHAN = 32


def draw_traces(key, part):
    subkeys = jax.random.split(key, 6)
    sample_index = jnp.arange(SAMPLES, dtype=jnp.int32)
    window_index = sample_index // HOP
    noise_field = jnp.clip(jax.random.normal(subkeys[0], (CHANNELS, SAMPLES), jnp.float32), -6.0, 6.0)
    tone_bottom = 1.0
    tone_top = 10.0
    ramp_index = jnp.arange(WINDOWS, dtype=jnp.int32).astype(jnp.float32)
    window_scale = 10.0 ** jax.random.uniform(subkeys[1], (WINDOWS,), jnp.float32)
    window_scale = window_scale * (1.0 + 2.0 * ramp_index / max(WINDOWS - 1, 1))
    per_sample = window_scale[window_index]
    channel_scale = 10.0 ** jax.random.uniform(subkeys[2], (CHANNELS, 1), jnp.float32)
    tone_bin = jax.random.randint(subkeys[3], (CHANNELS, 1), 1, NS // 2)
    tone_amp = jnp.exp(jax.random.uniform(subkeys[4], (CHANNELS, 1), jnp.float32, math.log(tone_bottom), math.log(tone_top)))
    tone_phase = jax.random.uniform(subkeys[5], (CHANNELS, WINDOWS), jnp.float32, -math.pi, math.pi)[:, window_index]
    cycle_index = tone_bin * sample_index[None, :] % NS
    tone_field = tone_amp * jnp.cos(cycle_index.astype(jnp.float32) * (2.0 * math.pi / NS) + tone_phase)
    return (channel_scale * (per_sample[None, :] * noise_field + tone_field)).astype(jnp.bfloat16)


def draw_kept_bins(key, part):
    middle = jax.random.permutation(key, NS // 2 - 3)[:KEEP - 2].astype(jnp.int32) + 2
    chosen = jnp.concatenate([jnp.array([1, NS // 2 - 1], dtype=jnp.int32), middle])
    return jnp.sort(chosen)


def draw_round_masks(key, part):
    subkeys = jax.random.split(key, 2)
    others = jax.random.permutation(subkeys[0], N_CHAN - 2)[:ROUNDS - 1].astype(jnp.int32) + 1
    round_list = jnp.concatenate([others, jnp.array([N_CHAN - 1], dtype=jnp.int32)])
    return jnp.roll(round_list, jax.random.randint(subkeys[1], (), 0, ROUNDS))


def setup_inputs(seed: int = 0) -> dict:
    arg_keys = jax.random.split(jax.random.key(seed), 4)
    traces = draw_traces(jax.random.fold_in(arg_keys[3], 71), 0)
    kept_bins = draw_kept_bins(jax.random.fold_in(arg_keys[3], 71), 0)
    round_masks = draw_round_masks(jax.random.fold_in(arg_keys[3], 71), 0)
    return {"traces": traces, "kept_bins": kept_bins, "round_masks": round_masks}


EPSILON = 1e-06

def dft_table(kept_bins):
    sample_index = jnp.arange(NS, dtype=jnp.int32)
    phase_index = kept_bins[:, None] * sample_index[None, :] % NS
    angles = phase_index.astype(jnp.float32) * jnp.float32(2.0 * math.pi / NS)
    hann_taper = 0.5 - 0.5 * jnp.cos(sample_index.astype(jnp.float32) * jnp.float32(2.0 * math.pi / NS))
    stacked = jnp.stack([hann_taper * jnp.cos(angles), -hann_taper * jnp.sin(angles)], axis=1)
    return stacked.reshape(kept_bins.shape[0] * 2, NS).astype(jnp.bfloat16)

def block_whitened(channel_block, transform):
    padded = jnp.concatenate([channel_block, jnp.zeros((CH, HOP), channel_block.dtype)], axis=1)
    padded = padded.reshape(CH, WINDOWS + 1, HOP).astype(jnp.float32)
    transform_f = transform.astype(jnp.float32)
    spectra = jnp.einsum('kn,cjn->kjc', transform_f[:, :HOP], padded[:, :-1])
    spectra = spectra + jnp.einsum('kn,cjn->kjc', transform_f[:, HOP:], padded[:, 1:])
    rounded = lax.optimization_barrier(spectra.astype(jnp.bfloat16))
    values = rounded.astype(jnp.float32).reshape(KEEP, 2, WINDOWS, CH)
    power_mean = lax.optimization_barrier(jnp.sum(values * values, axis=(1, 2))) / WINDOWS
    return (values * lax.rsqrt(power_mean + EPSILON)[:, None, None, :]).astype(jnp.bfloat16)

def correlate(left_block, right_block):
    left_f = left_block.astype(jnp.float32)
    right_f = right_block.astype(jnp.float32)
    products = jnp.einsum('kpwc,kqwd->kpqcd', left_f, right_f)
    real_part = products[:, 0, 0] + products[:, 1, 1]
    imag_part = products[:, 1, 0] - products[:, 0, 1]
    return jnp.stack([real_part, imag_part], axis=1) * (1.0 / math.sqrt(WINDOWS))

def arrange(stacked):
    return jnp.transpose(stacked, (1, 2, 0, 3, 4)).reshape(KEEP, 2, CHANNELS, CH)

def reference(traces, kept_bins, round_masks):
    transform = dft_table(kept_bins)
    blocks = traces.reshape(N_CHAN, CH, SAMPLES)
    whitened = lax.map(lambda channel_block: block_whitened(channel_block, transform), blocks)
    indices = jnp.arange(N_CHAN, dtype=jnp.int32)
    auto_terms = lax.map(lambda block_index: correlate(whitened[block_index], whitened[block_index]), indices)
    crosses = []
    for round_no in range(ROUNDS):
        round_mask = round_masks[round_no]
        paired = lax.map(lambda block_index: correlate(whitened[block_index], whitened[jnp.bitwise_xor(block_index, round_mask)]), indices)
        crosses.append(arrange(paired))
    return (jnp.stack(crosses), arrange(auto_terms))
```

```python
import functools
import math

import jax
import jax.numpy as jnp
from jax import lax
from jax.sharding import PartitionSpec as P

NS = 512
ROUNDS = 2


EPSILON = 1e-06


def shifted(block, axis, distance):
    devices = range(lax.axis_size(axis))
    route = [(i - distance, i) for i in devices if i - distance in devices]
    return lax.ppermute(block, axis, route)


def xor_moved(block, axis, mask):
    return lax.ppermute(block, axis, [(i, i ^ mask) for i in range(lax.axis_size(axis))])


def dft_table(kept_bins):
    sample_index = jnp.arange(NS, dtype=jnp.int32)
    phase_index = kept_bins[:, None] * sample_index[None, :] % NS
    angles = phase_index.astype(jnp.float32) * jnp.float32(2.0 * math.pi / NS)
    hann_taper = 0.5 - 0.5 * jnp.cos(
        sample_index.astype(jnp.float32) * jnp.float32(2.0 * math.pi / NS)
    )
    stacked = jnp.stack([hann_taper * jnp.cos(angles), -hann_taper * jnp.sin(angles)], axis=1)
    return stacked.reshape(kept_bins.shape[0] * 2, NS).astype(jnp.bfloat16)


def correlate(left_block, right_block, windows):
    products = jnp.einsum(
        "kpwc,kqwd->kpqcd", left_block, right_block, preferred_element_type=jnp.float32
    )
    real_part = products[:, 0, 0] + products[:, 1, 1]
    imag_part = products[:, 1, 0] - products[:, 0, 1]
    return jnp.stack([real_part, imag_part], axis=1) * (1.0 / math.sqrt(windows))


def body(traces, kept_bins, round_masks):
    channels, samples_here = traces.shape
    hop_length = NS // 2
    frames = samples_here // hop_length
    keep_count = kept_bins.shape[0]
    transform = dft_table(kept_bins)
    following = shifted(traces[:, :hop_length], "freq", -1)
    extended = jnp.concatenate([traces, following], axis=1).reshape(
        channels, frames + 1, hop_length
    )
    spectra = jnp.einsum(
        "kn,cjn->kjc",
        transform[:, :hop_length],
        extended[:, :-1],
        preferred_element_type=jnp.float32,
    )
    spectra = spectra + jnp.einsum(
        "kn,cjn->kjc",
        transform[:, hop_length:],
        extended[:, 1:],
        preferred_element_type=jnp.float32,
    )
    rounded = spectra.astype(jnp.bfloat16).reshape(keep_count, 2, frames * channels)
    windows = frames * lax.axis_size("freq")
    arrived_bins = lax.all_to_all(rounded, "freq", split_axis=0, concat_axis=2, tiled=True)
    values = arrived_bins.astype(jnp.float32).reshape(-1, 2, windows, channels)
    power_mean = jnp.sum(values * values, axis=(1, 2)) / windows
    own_block = (values * lax.rsqrt(power_mean + EPSILON)[:, None, None, :]).astype(jnp.bfloat16)
    auto_spectra = correlate(own_block, own_block, windows)
    blocks_count = lax.axis_size("chan")
    branches = [
        functools.partial(xor_moved, axis="chan", mask=mask) for mask in range(1, blocks_count)
    ]
    crosses = []
    for round_no in range(ROUNDS):
        which = jnp.clip(round_masks[round_no] - 1, 0, blocks_count - 2)
        partner = lax.switch(which, branches, own_block)
        crosses.append(correlate(own_block, partner, windows))
    return (jnp.stack(crosses), auto_spectra)


def solution(mesh):
    placed = (P("chan", "freq"), P(), P())
    return jax.shard_map(
        body,
        mesh=mesh,
        in_specs=placed,
        out_specs=(P(None, "freq", None, "chan", None), P("freq", None, "chan", None)),
        check_vma=False,
    )
```

```python
import functools
import math

import jax
import jax.numpy as jnp
from jax import lax
from jax.sharding import PartitionSpec as P

NS = 512


EPSILON = 1e-06


def shifted(block, axis, distance):
    devices = range(lax.axis_size(axis))
    route = [(i - distance, i) for i in devices if i - distance in devices]
    return lax.ppermute(block, axis, route)


def xor_moved(block, axis, mask):
    return lax.ppermute(block, axis, [(i, i ^ mask) for i in range(lax.axis_size(axis))])


def dft_table(kept_bins):
    sample_index = jnp.arange(NS, dtype=jnp.int32)
    phase_index = kept_bins[:, None] * sample_index[None, :] % NS
    angles = phase_index.astype(jnp.float32) * jnp.float32(2.0 * math.pi / NS)
    hann_taper = 0.5 - 0.5 * jnp.cos(
        sample_index.astype(jnp.float32) * jnp.float32(2.0 * math.pi / NS)
    )
    stacked = jnp.stack([hann_taper * jnp.cos(angles), -hann_taper * jnp.sin(angles)], axis=1)
    return stacked.reshape(kept_bins.shape[0] * 2, NS).astype(jnp.bfloat16)


def correlate(left_block, right_block, windows):
    products = jnp.einsum(
        "kpwc,kqwd->kpqcd", left_block, right_block, preferred_element_type=jnp.float32
    )
    real_part = products[:, 0, 0] + products[:, 1, 1]
    imag_part = products[:, 1, 0] - products[:, 0, 1]
    return jnp.stack([real_part, imag_part], axis=1) * (1.0 / math.sqrt(windows))


def body(traces, kept_bins, round_masks):
    channels, samples_here = traces.shape
    hop_length = NS // 2
    frames = samples_here // hop_length
    keep_count = kept_bins.shape[0]
    transform = dft_table(kept_bins)
    following = shifted(traces[:, :hop_length], "freq", -1)
    extended = jnp.concatenate([traces, following], axis=1).reshape(
        channels, frames + 1, hop_length
    )
    spectra = jnp.einsum(
        "kn,cjn->kjc",
        transform[:, :hop_length],
        extended[:, :-1],
        preferred_element_type=jnp.float32,
    )
    spectra = spectra + jnp.einsum(
        "kn,cjn->kjc",
        transform[:, hop_length:],
        extended[:, 1:],
        preferred_element_type=jnp.float32,
    )
    rounded = spectra.astype(jnp.bfloat16).reshape(keep_count, 2, frames * channels)
    windows = frames * lax.axis_size("freq")
    arrived_bins = lax.all_to_all(rounded, "freq", split_axis=0, concat_axis=2, tiled=True)
    values = arrived_bins.astype(jnp.float32).reshape(-1, 2, windows, channels)
    power_mean = jnp.sum(values * values, axis=(1, 2)) / windows
    own_block = (values * lax.rsqrt(power_mean + EPSILON)[:, None, None, :]).astype(jnp.bfloat16)
    auto_spectra = correlate(own_block, own_block, windows)
    blocks_count = lax.axis_size("chan")
    branches = [
        functools.partial(xor_moved, axis="chan", mask=mask) for mask in range(1, blocks_count)
    ]
    half = own_block.shape[0] // 2
    block_index = lax.axis_index("chan")

    def one_round(carry, round_mask):
        which = jnp.clip(round_mask - 1, 0, blocks_count - 2)
        top_shift = sum((round_mask >> level) > 1 for level in range(blocks_count.bit_length()))
        upper = jnp.right_shift(block_index, top_shift) % 2
        kept = lax.dynamic_slice_in_dim(own_block, upper * half, half, axis=0)
        given = lax.dynamic_slice_in_dim(own_block, (1 - upper) * half, half, axis=0)
        partner_kept = lax.switch(which, branches, given)
        mine = correlate(kept, partner_kept, windows)
        theirs = jnp.stack([mine[:, 0], -mine[:, 1]], axis=1).swapaxes(2, 3)
        returned = lax.switch(which, branches, theirs.astype(jnp.bfloat16)).astype(jnp.float32)
        lower_first = jnp.concatenate([mine, returned], axis=0)
        upper_first = jnp.concatenate([returned, mine], axis=0)
        return carry, jnp.where(upper == 0, lower_first, upper_first)

    crosses = lax.scan(one_round, 0, round_masks)[1]
    return (crosses, auto_spectra)


def solution(mesh):
    placed = (P("chan", "freq"), P(), P())
    return jax.shard_map(
        body,
        mesh=mesh,
        in_specs=placed,
        out_specs=(P(None, "freq", None, "chan", None), P("freq", None, "chan", None)),
        check_vma=False,
    )
```

```python
import functools
import math

import jax
import jax.numpy as jnp
from jax import lax
from jax.sharding import PartitionSpec as P

NS = 512


EPSILON = 1e-06


def shifted(block, axis, distance):
    devices = range(lax.axis_size(axis))
    route = [(i - distance, i) for i in devices if i - distance in devices]
    return lax.ppermute(block, axis, route)


def xor_moved(block, axis, mask):
    return lax.ppermute(block, axis, [(i, i ^ mask) for i in range(lax.axis_size(axis))])


def dft_table(kept_bins):
    sample_index = jnp.arange(NS, dtype=jnp.int32)
    phase_index = kept_bins[:, None] * sample_index[None, :] % NS
    angles = phase_index.astype(jnp.float32) * jnp.float32(2.0 * math.pi / NS)
    hann_taper = 0.5 - 0.5 * jnp.cos(
        sample_index.astype(jnp.float32) * jnp.float32(2.0 * math.pi / NS)
    )
    stacked = jnp.stack([hann_taper * jnp.cos(angles), -hann_taper * jnp.sin(angles)], axis=1)
    return stacked.reshape(kept_bins.shape[0] * 2, NS).astype(jnp.bfloat16)


def correlate(left_block, right_block, windows):
    products = jnp.einsum(
        "fkpjc,fkqjd->kpqcd", left_block, right_block, preferred_element_type=jnp.float32
    )
    real_part = products[:, 0, 0] + products[:, 1, 1]
    imag_part = products[:, 1, 0] - products[:, 0, 1]
    return jnp.stack([real_part, imag_part], axis=1) * (1.0 / math.sqrt(windows))


def body(traces, kept_bins, round_masks):
    channels, samples_here = traces.shape
    hop_length = NS // 2
    frames = samples_here // hop_length
    keep_count = kept_bins.shape[0]
    transform = dft_table(kept_bins)
    following = shifted(traces[:, :hop_length], "freq", -1)
    extended = jnp.concatenate([traces, following], axis=1).reshape(
        channels, frames + 1, hop_length
    )
    spectra = jnp.einsum(
        "kn,cjn->kjc",
        transform[:, :hop_length],
        extended[:, :-1],
        preferred_element_type=jnp.float32,
    )
    spectra = spectra + jnp.einsum(
        "kn,cjn->kjc",
        transform[:, hop_length:],
        extended[:, 1:],
        preferred_element_type=jnp.float32,
    )
    sources = lax.axis_size("freq")
    rounded = spectra.astype(jnp.bfloat16).reshape(sources, -1, 2, frames, channels)
    windows = frames * sources
    arrived_bins = lax.all_to_all(rounded, "freq", split_axis=0, concat_axis=0, tiled=True)
    values = arrived_bins.astype(jnp.float32)
    power_mean = jnp.sum(values * values, axis=(0, 2, 3)) / windows
    own_block = (values * lax.rsqrt(power_mean + EPSILON)[:, None, None, :]).astype(jnp.bfloat16)
    auto_spectra = correlate(own_block, own_block, windows)
    blocks_count = lax.axis_size("chan")
    branches = [
        functools.partial(xor_moved, axis="chan", mask=mask) for mask in range(1, blocks_count)
    ]
    half = own_block.shape[1] // 2
    block_index = lax.axis_index("chan")

    def one_round(carry, round_mask):
        which = jnp.clip(round_mask - 1, 0, blocks_count - 2)
        top_shift = sum((round_mask >> level) > 1 for level in range(blocks_count.bit_length()))
        upper = jnp.right_shift(block_index, top_shift) % 2
        kept = lax.dynamic_slice_in_dim(own_block, upper * half, half, axis=1)
        given = lax.dynamic_slice_in_dim(own_block, (1 - upper) * half, half, axis=1)
        partner_kept = lax.switch(which, branches, given)
        mine = correlate(kept, partner_kept, windows)
        theirs = jnp.stack([mine[:, 0], -mine[:, 1]], axis=1).swapaxes(2, 3)
        returned = lax.switch(which, branches, theirs.astype(jnp.bfloat16)).astype(jnp.float32)
        lower_first = jnp.concatenate([mine, returned], axis=0)
        upper_first = jnp.concatenate([returned, mine], axis=0)
        return carry, jnp.where(upper == 0, lower_first, upper_first)

    crosses = lax.scan(one_round, 0, round_masks)[1]
    return (crosses, auto_spectra)


def solution(mesh):
    placed = (P("chan", "freq"), P(), P())
    return jax.shard_map(
        body,
        mesh=mesh,
        in_specs=placed,
        out_specs=(P(None, "freq", None, "chan", None), P("freq", None, "chan", None)),
        check_vma=False,
    )
```

```python
import functools
import math

import jax
import jax.numpy as jnp
from jax import lax
from jax.sharding import PartitionSpec as P

NS = 512


EPSILON = 1e-06


def shifted(block, axis, distance):
    devices = range(lax.axis_size(axis))
    route = [(i - distance, i) for i in devices if i - distance in devices]
    return lax.ppermute(block, axis, route)


def xor_moved(block, axis, mask):
    return lax.ppermute(block, axis, [(i, i ^ mask) for i in range(lax.axis_size(axis))])


def dft_table(kept_bins):
    sample_index = jnp.arange(NS, dtype=jnp.int32)
    phase_index = kept_bins[:, None] * sample_index[None, :] % NS
    angles = phase_index.astype(jnp.float32) * jnp.float32(2.0 * math.pi / NS)
    hann_taper = 0.5 - 0.5 * jnp.cos(
        sample_index.astype(jnp.float32) * jnp.float32(2.0 * math.pi / NS)
    )
    stacked = jnp.stack([hann_taper * jnp.cos(angles), -hann_taper * jnp.sin(angles)], axis=1)
    return stacked.reshape(kept_bins.shape[0] * 2, NS).astype(jnp.bfloat16)


def correlate(left_block, right_block, windows):
    products = jnp.einsum(
        "fkpjc,fkqjd->kpqcd", left_block, right_block, preferred_element_type=jnp.float32
    )
    real_part = products[:, 0, 0] + products[:, 1, 1]
    imag_part = products[:, 1, 0] - products[:, 0, 1]
    return jnp.stack([real_part, imag_part], axis=1) * (1.0 / math.sqrt(windows))


def body(traces, kept_bins, round_masks):
    channels, samples_here = traces.shape
    hop_length = NS // 2
    frames = samples_here // hop_length
    keep_count = kept_bins.shape[0]
    transform = dft_table(kept_bins)
    following = shifted(traces[:, :hop_length], "freq", -1)
    extended = jnp.concatenate([traces, following], axis=1).reshape(
        channels, frames + 1, hop_length
    )
    spectra = jnp.einsum(
        "kn,cjn->kjc",
        transform[:, :hop_length],
        extended[:, :-1],
        preferred_element_type=jnp.float32,
    )
    spectra = spectra + jnp.einsum(
        "kn,cjn->kjc",
        transform[:, hop_length:],
        extended[:, 1:],
        preferred_element_type=jnp.float32,
    )
    sources = lax.axis_size("freq")
    windows = frames * sources
    rounded = spectra.astype(jnp.bfloat16).reshape(sources, -1, 2, frames, channels)
    half = rounded.shape[1] // 2
    blocks_count = lax.axis_size("chan")
    block_index = lax.axis_index("chan")
    rounds = round_masks.shape[0]

    def upper_of(round_mask):
        top_shift = sum((round_mask >> level) > 1 for level in range(blocks_count.bit_length()))
        return jnp.right_shift(block_index, top_shift) % 2

    def regrouped(part):
        return lax.all_to_all(part, "freq", split_axis=0, concat_axis=0, tiled=True)

    def whitened(arrived):
        values = arrived.astype(jnp.float32)
        power_mean = jnp.sum(values * values, axis=(0, 2, 3)) / windows
        return (values * lax.rsqrt(power_mean + EPSILON)[:, None, None, :]).astype(jnp.bfloat16)

    def moved_and_regrouped(parts, mask):
        sent, local = parts
        return xor_moved(sent, "chan", mask), regrouped(local)

    branches = [
        functools.partial(xor_moved, axis="chan", mask=mask) for mask in range(1, blocks_count)
    ]
    first_branches = [
        functools.partial(moved_and_regrouped, mask=mask) for mask in range(1, blocks_count)
    ]
    upper = upper_of(round_masks[0])
    given = whitened(regrouped(lax.dynamic_slice_in_dim(rounded, (1 - upper) * half, half, axis=1)))
    crosses = []
    for round_no in range(rounds):
        round_mask = round_masks[round_no]
        which = jnp.clip(round_mask - 1, 0, blocks_count - 2)
        if round_no == 0:
            local = lax.dynamic_slice_in_dim(rounded, upper * half, half, axis=1)
            partner_kept, arrived = lax.switch(which, first_branches, (given, local))
            kept = whitened(arrived)
            own_block = jnp.where(
                upper == 0,
                jnp.concatenate([kept, given], axis=1),
                jnp.concatenate([given, kept], axis=1),
            )
        else:
            upper = upper_of(round_mask)
            kept = lax.dynamic_slice_in_dim(own_block, upper * half, half, axis=1)
            given = lax.dynamic_slice_in_dim(own_block, (1 - upper) * half, half, axis=1)
            partner_kept = lax.switch(which, branches, given)
        mine = correlate(kept, partner_kept, windows)
        theirs = jnp.stack([mine[:, 0], -mine[:, 1]], axis=1).swapaxes(2, 3)
        returned = lax.switch(which, branches, theirs.astype(jnp.bfloat16)).astype(jnp.float32)
        crosses.append(
            jnp.where(
                upper == 0,
                jnp.concatenate([mine, returned], axis=0),
                jnp.concatenate([returned, mine], axis=0),
            )
        )
    auto_spectra = correlate(own_block, own_block, windows)
    return (jnp.stack(crosses), auto_spectra)


def solution(mesh):
    placed = (P("chan", "freq"), P(), P())
    return jax.shard_map(
        body,
        mesh=mesh,
        in_specs=placed,
        out_specs=(P(None, "freq", None, "chan", None), P("freq", None, "chan", None)),
        check_vma=False,
    )
```

```python
import functools
import math

import jax
import jax.numpy as jnp
from jax import lax
from jax.sharding import PartitionSpec as P

NS = 512


EPSILON = 1e-06


def shifted(block, axis, distance):
    devices = range(lax.axis_size(axis))
    route = [(i - distance, i) for i in devices if i - distance in devices]
    return lax.ppermute(block, axis, route)


def xor_moved(block, axis, mask):
    return lax.ppermute(block, axis, [(i, i ^ mask) for i in range(lax.axis_size(axis))])


def dft_table(kept_bins):
    sample_index = jnp.arange(NS, dtype=jnp.int32)
    phase_index = kept_bins[:, None] * sample_index[None, :] % NS
    angles = phase_index.astype(jnp.float32) * jnp.float32(2.0 * math.pi / NS)
    hann_taper = 0.5 - 0.5 * jnp.cos(
        sample_index.astype(jnp.float32) * jnp.float32(2.0 * math.pi / NS)
    )
    stacked = jnp.stack([hann_taper * jnp.cos(angles), -hann_taper * jnp.sin(angles)], axis=1)
    return stacked.reshape(kept_bins.shape[0] * 2, NS).astype(jnp.bfloat16)


def correlate(left_block, right_block, windows):
    products = jnp.einsum(
        "fkpjc,fkqjd->kpqcd", left_block, right_block, preferred_element_type=jnp.float32
    )
    real_part = products[:, 0, 0] + products[:, 1, 1]
    imag_part = products[:, 1, 0] - products[:, 0, 1]
    return jnp.stack([real_part, imag_part], axis=1) * (1.0 / math.sqrt(windows))


def body(traces, kept_bins, round_masks):
    channels, samples_here = traces.shape
    hop_length = NS // 2
    frames = samples_here // hop_length
    keep_count = kept_bins.shape[0]
    transform = dft_table(kept_bins)
    following = shifted(traces[:, :hop_length], "freq", -1)
    extended = jnp.concatenate([traces, following], axis=1).reshape(
        channels, frames + 1, hop_length
    )
    spectra = jnp.einsum(
        "kn,cjn->kjc",
        transform[:, :hop_length],
        extended[:, :-1],
        preferred_element_type=jnp.float32,
    )
    spectra = spectra + jnp.einsum(
        "kn,cjn->kjc",
        transform[:, hop_length:],
        extended[:, 1:],
        preferred_element_type=jnp.float32,
    )
    sources = lax.axis_size("freq")
    rounded = spectra.astype(jnp.bfloat16).reshape(sources, -1, 2, frames, channels)
    windows = frames * sources
    arrived_bins = lax.all_to_all(rounded, "freq", split_axis=0, concat_axis=0, tiled=True)
    values = arrived_bins.astype(jnp.float32)
    power_mean = jnp.sum(values * values, axis=(0, 2, 3)) / windows
    own_block = (values * lax.rsqrt(power_mean + EPSILON)[:, None, None, :]).astype(jnp.bfloat16)
    auto_spectra = correlate(own_block, own_block, windows)
    blocks_count = lax.axis_size("chan")
    branches = [
        functools.partial(xor_moved, axis="chan", mask=mask) for mask in range(1, blocks_count)
    ]
    half = own_block.shape[1] // 2
    block_index = lax.axis_index("chan")

    crosses = []
    for round_no in range(round_masks.shape[0]):
        round_mask = round_masks[round_no]
        which = jnp.clip(round_mask - 1, 0, blocks_count - 2)
        top_shift = sum((round_mask >> level) > 1 for level in range(blocks_count.bit_length()))
        upper = jnp.right_shift(block_index, top_shift) % 2
        kept = lax.dynamic_slice_in_dim(own_block, upper * half, half, axis=1)
        given = lax.dynamic_slice_in_dim(own_block, (1 - upper) * half, half, axis=1)
        partner_kept = lax.switch(which, branches, given)
        mine = correlate(kept, partner_kept, windows)
        theirs = jnp.stack([mine[:, 0], -mine[:, 1]], axis=1).swapaxes(2, 3)
        returned = lax.switch(which, branches, theirs.astype(jnp.bfloat16)).astype(jnp.float32)
        lower_first = jnp.concatenate([mine, returned], axis=0)
        upper_first = jnp.concatenate([returned, mine], axis=0)
        crosses.append(jnp.where(upper == 0, lower_first, upper_first))
    return (jnp.stack(crosses), auto_spectra)


def solution(mesh):
    placed = (P("chan", "freq"), P(), P())
    return jax.shard_map(
        body,
        mesh=mesh,
        in_specs=placed,
        out_specs=(P(None, "freq", None, "chan", None), P("freq", None, "chan", None)),
        check_vma=False,
    )
```

```python
import functools
import math

import jax
import jax.numpy as jnp
from jax import lax
from jax.sharding import PartitionSpec as P

NS = 512


EPSILON = 1e-06


def shifted(block, axis, distance):
    devices = range(lax.axis_size(axis))
    route = [(i - distance, i) for i in devices if i - distance in devices]
    return lax.ppermute(block, axis, route)


def xor_moved(block, axis, mask):
    return lax.ppermute(block, axis, [(i, i ^ mask) for i in range(lax.axis_size(axis))])


def dft_table(kept_bins):
    sample_index = jnp.arange(NS, dtype=jnp.int32)
    phase_index = kept_bins[:, None] * sample_index[None, :] % NS
    angles = phase_index.astype(jnp.float32) * jnp.float32(2.0 * math.pi / NS)
    hann_taper = 0.5 - 0.5 * jnp.cos(
        sample_index.astype(jnp.float32) * jnp.float32(2.0 * math.pi / NS)
    )
    stacked = jnp.stack([hann_taper * jnp.cos(angles), -hann_taper * jnp.sin(angles)], axis=1)
    return stacked.reshape(kept_bins.shape[0] * 2, NS).astype(jnp.bfloat16)


def correlate(left_block, right_block, windows):
    products = jnp.einsum(
        "fkpjc,fkqjd->kpqcd", left_block, right_block, preferred_element_type=jnp.float32
    )
    real_part = products[:, 0, 0] + products[:, 1, 1]
    imag_part = products[:, 1, 0] - products[:, 0, 1]
    return jnp.stack([real_part, imag_part], axis=1) * (1.0 / math.sqrt(windows))


def body(traces, kept_bins, round_masks):
    channels, samples_here = traces.shape
    hop_length = NS // 2
    frames = samples_here // hop_length
    keep_count = kept_bins.shape[0]
    transform = dft_table(kept_bins)
    following = shifted(traces[:, :hop_length], "freq", -1)
    extended = jnp.concatenate([traces, following], axis=1).reshape(
        channels, frames + 1, hop_length
    )
    spectra = jnp.einsum(
        "kn,cjn->kjc",
        transform[:, :hop_length],
        extended[:, :-1],
        preferred_element_type=jnp.float32,
    )
    spectra = spectra + jnp.einsum(
        "kn,cjn->kjc",
        transform[:, hop_length:],
        extended[:, 1:],
        preferred_element_type=jnp.float32,
    )
    sources = lax.axis_size("freq")
    rounded = spectra.astype(jnp.bfloat16).reshape(sources, -1, 2, frames, channels)
    windows = frames * sources
    arrived_bins = lax.all_to_all(rounded, "freq", split_axis=0, concat_axis=0, tiled=True)
    values = arrived_bins.astype(jnp.float32)
    power_mean = jnp.sum(values * values, axis=(0, 2, 3)) / windows
    own_block = (values * lax.rsqrt(power_mean + EPSILON)[:, None, None, :]).astype(jnp.bfloat16)
    auto_spectra = correlate(own_block, own_block, windows)
    blocks_count = lax.axis_size("chan")
    branches = [
        functools.partial(xor_moved, axis="chan", mask=mask) for mask in range(1, blocks_count)
    ]
    half = own_block.shape[1] // 2
    block_index = lax.axis_index("chan")

    def one_round(carry, round_mask):
        which = jnp.clip(round_mask - 1, 0, blocks_count - 2)
        top_shift = sum((round_mask >> level) > 1 for level in range(blocks_count.bit_length()))
        upper = jnp.right_shift(block_index, top_shift) % 2
        kept = lax.dynamic_slice_in_dim(own_block, upper * half, half, axis=1)
        given = lax.dynamic_slice_in_dim(own_block, (1 - upper) * half, half, axis=1)
        partner_kept = lax.switch(which, branches, given)
        mine = correlate(kept, partner_kept, windows)
        theirs = jnp.stack([mine[:, 0], -mine[:, 1]], axis=1).swapaxes(2, 3)
        returned = lax.switch(which, branches, theirs.astype(jnp.bfloat16)).astype(jnp.float32)
        lower_first = jnp.concatenate([mine, returned], axis=0)
        upper_first = jnp.concatenate([returned, mine], axis=0)
        return carry, jnp.where(upper == 0, lower_first, upper_first)

    order = jnp.argsort(round_masks)
    crosses = lax.scan(one_round, 0, round_masks[order])[1]
    crosses = jnp.take(crosses, jnp.argsort(order), axis=0)
    return (crosses, auto_spectra)


def solution(mesh):
    placed = (P("chan", "freq"), P(), P())
    return jax.shard_map(
        body,
        mesh=mesh,
        in_specs=placed,
        out_specs=(P(None, "freq", None, "chan", None), P("freq", None, "chan", None)),
        check_vma=False,
    )
```

```python
import functools
import math

import jax
import jax.numpy as jnp
from jax import lax
from jax.sharding import PartitionSpec as P

NS = 512


EPSILON = 1e-06


def shifted(block, axis, distance):
    devices = range(lax.axis_size(axis))
    route = [(i - distance, i) for i in devices if i - distance in devices]
    return lax.ppermute(block, axis, route)


def xor_moved(block, axis, mask):
    return lax.ppermute(block, axis, [(i, i ^ mask) for i in range(lax.axis_size(axis))])


def xor_moved_in_turn(block, axis, mask):
    split = block.shape[1] // 2
    first = xor_moved(block[:, :split], axis, mask)
    first, rest = lax.optimization_barrier((first, block[:, split:]))
    return jnp.concatenate([first, xor_moved(rest, axis, mask)], axis=1)


def dft_table(kept_bins):
    sample_index = jnp.arange(NS, dtype=jnp.int32)
    phase_index = kept_bins[:, None] * sample_index[None, :] % NS
    angles = phase_index.astype(jnp.float32) * jnp.float32(2.0 * math.pi / NS)
    hann_taper = 0.5 - 0.5 * jnp.cos(
        sample_index.astype(jnp.float32) * jnp.float32(2.0 * math.pi / NS)
    )
    stacked = jnp.stack([hann_taper * jnp.cos(angles), -hann_taper * jnp.sin(angles)], axis=1)
    return stacked.reshape(kept_bins.shape[0] * 2, NS).astype(jnp.bfloat16)


def correlate(left_block, right_block, windows):
    products = jnp.einsum(
        "fkpjc,fkqjd->kpqcd", left_block, right_block, preferred_element_type=jnp.float32
    )
    real_part = products[:, 0, 0] + products[:, 1, 1]
    imag_part = products[:, 1, 0] - products[:, 0, 1]
    return jnp.stack([real_part, imag_part], axis=1) * (1.0 / math.sqrt(windows))


def body(traces, kept_bins, round_masks):
    channels, samples_here = traces.shape
    hop_length = NS // 2
    frames = samples_here // hop_length
    keep_count = kept_bins.shape[0]
    transform = dft_table(kept_bins)
    following = shifted(traces[:, :hop_length], "freq", -1)
    extended = jnp.concatenate([traces, following], axis=1).reshape(
        channels, frames + 1, hop_length
    )
    spectra = jnp.einsum(
        "kn,cjn->kjc",
        transform[:, :hop_length],
        extended[:, :-1],
        preferred_element_type=jnp.float32,
    )
    spectra = spectra + jnp.einsum(
        "kn,cjn->kjc",
        transform[:, hop_length:],
        extended[:, 1:],
        preferred_element_type=jnp.float32,
    )
    sources = lax.axis_size("freq")
    rounded = spectra.astype(jnp.bfloat16).reshape(sources, -1, 2, frames, channels)
    windows = frames * sources
    arrived_bins = lax.all_to_all(rounded, "freq", split_axis=0, concat_axis=0, tiled=True)
    values = arrived_bins.astype(jnp.float32)
    power_mean = jnp.sum(values * values, axis=(0, 2, 3)) / windows
    own_block = (values * lax.rsqrt(power_mean + EPSILON)[:, None, None, :]).astype(jnp.bfloat16)
    auto_spectra = correlate(own_block, own_block, windows)
    blocks_count = lax.axis_size("chan")
    branches = [
        functools.partial(xor_moved, axis="chan", mask=mask) for mask in range(1, blocks_count)
    ]
    half = own_block.shape[1] // 2
    spectra_branches = [
        functools.partial(xor_moved_in_turn, axis="chan", mask=mask)
        for mask in range(1, blocks_count)
    ]
    block_index = lax.axis_index("chan")

    def one_round(carry, round_mask):
        which = jnp.clip(round_mask - 1, 0, blocks_count - 2)
        top_shift = sum((round_mask >> level) > 1 for level in range(blocks_count.bit_length()))
        upper = jnp.right_shift(block_index, top_shift) % 2
        kept = lax.dynamic_slice_in_dim(own_block, upper * half, half, axis=1)
        given = lax.dynamic_slice_in_dim(own_block, (1 - upper) * half, half, axis=1)
        partner_kept = lax.switch(which, spectra_branches, given)
        mine = correlate(kept, partner_kept, windows)
        theirs = jnp.stack([mine[:, 0], -mine[:, 1]], axis=1).swapaxes(2, 3)
        returned = lax.switch(which, branches, theirs.astype(jnp.bfloat16)).astype(jnp.float32)
        lower_first = jnp.concatenate([mine, returned], axis=0)
        upper_first = jnp.concatenate([returned, mine], axis=0)
        return carry, jnp.where(upper == 0, lower_first, upper_first)

    crosses = lax.scan(one_round, 0, round_masks)[1]
    return (crosses, auto_spectra)


def solution(mesh):
    placed = (P("chan", "freq"), P(), P())
    return jax.shard_map(
        body,
        mesh=mesh,
        in_specs=placed,
        out_specs=(P(None, "freq", None, "chan", None), P("freq", None, "chan", None)),
        check_vma=False,
    )
```

```python
import functools
import math

import jax
import jax.numpy as jnp
from jax import lax
from jax.sharding import PartitionSpec as P

NS = 512


EPSILON = 1e-06


def shifted(block, axis, distance):
    devices = range(lax.axis_size(axis))
    route = [(i - distance, i) for i in devices if i - distance in devices]
    return lax.ppermute(block, axis, route)


def xor_moved(block, axis, mask):
    return lax.ppermute(block, axis, [(i, i ^ mask) for i in range(lax.axis_size(axis))])


def xor_moved_after_probe(block, axis, mask):
    probe = xor_moved(block[:1, :1, :1, :1, :], axis, mask)
    probe, block = lax.optimization_barrier((probe, block))
    moved = xor_moved(block, axis, mask)
    return moved + (probe[:1, :1, :1, :1, :1] * 0).astype(moved.dtype)


def dft_table(kept_bins):
    sample_index = jnp.arange(NS, dtype=jnp.int32)
    phase_index = kept_bins[:, None] * sample_index[None, :] % NS
    angles = phase_index.astype(jnp.float32) * jnp.float32(2.0 * math.pi / NS)
    hann_taper = 0.5 - 0.5 * jnp.cos(
        sample_index.astype(jnp.float32) * jnp.float32(2.0 * math.pi / NS)
    )
    stacked = jnp.stack([hann_taper * jnp.cos(angles), -hann_taper * jnp.sin(angles)], axis=1)
    return stacked.reshape(kept_bins.shape[0] * 2, NS).astype(jnp.bfloat16)


def correlate(left_block, right_block, windows):
    products = jnp.einsum(
        "fkpjc,fkqjd->kpqcd", left_block, right_block, preferred_element_type=jnp.float32
    )
    real_part = products[:, 0, 0] + products[:, 1, 1]
    imag_part = products[:, 1, 0] - products[:, 0, 1]
    return jnp.stack([real_part, imag_part], axis=1) * (1.0 / math.sqrt(windows))


def body(traces, kept_bins, round_masks):
    channels, samples_here = traces.shape
    hop_length = NS // 2
    frames = samples_here // hop_length
    keep_count = kept_bins.shape[0]
    transform = dft_table(kept_bins)
    following = shifted(traces[:, :hop_length], "freq", -1)
    extended = jnp.concatenate([traces, following], axis=1).reshape(
        channels, frames + 1, hop_length
    )
    spectra = jnp.einsum(
        "kn,cjn->kjc",
        transform[:, :hop_length],
        extended[:, :-1],
        preferred_element_type=jnp.float32,
    )
    spectra = spectra + jnp.einsum(
        "kn,cjn->kjc",
        transform[:, hop_length:],
        extended[:, 1:],
        preferred_element_type=jnp.float32,
    )
    sources = lax.axis_size("freq")
    rounded = spectra.astype(jnp.bfloat16).reshape(sources, -1, 2, frames, channels)
    windows = frames * sources
    arrived_bins = lax.all_to_all(rounded, "freq", split_axis=0, concat_axis=0, tiled=True)
    values = arrived_bins.astype(jnp.float32)
    power_mean = jnp.sum(values * values, axis=(0, 2, 3)) / windows
    own_block = (values * lax.rsqrt(power_mean + EPSILON)[:, None, None, :]).astype(jnp.bfloat16)
    auto_spectra = correlate(own_block, own_block, windows)
    blocks_count = lax.axis_size("chan")
    branches = [
        functools.partial(xor_moved, axis="chan", mask=mask) for mask in range(1, blocks_count)
    ]
    half = own_block.shape[1] // 2
    spectra_branches = [
        functools.partial(xor_moved_after_probe, axis="chan", mask=mask)
        for mask in range(1, blocks_count)
    ]
    block_index = lax.axis_index("chan")

    def one_round(carry, round_mask):
        which = jnp.clip(round_mask - 1, 0, blocks_count - 2)
        top_shift = sum((round_mask >> level) > 1 for level in range(blocks_count.bit_length()))
        upper = jnp.right_shift(block_index, top_shift) % 2
        kept = lax.dynamic_slice_in_dim(own_block, upper * half, half, axis=1)
        given = lax.dynamic_slice_in_dim(own_block, (1 - upper) * half, half, axis=1)
        partner_kept = lax.switch(which, spectra_branches, given)
        mine = correlate(kept, partner_kept, windows)
        theirs = jnp.stack([mine[:, 0], -mine[:, 1]], axis=1).swapaxes(2, 3)
        returned = lax.switch(which, branches, theirs.astype(jnp.bfloat16)).astype(jnp.float32)
        lower_first = jnp.concatenate([mine, returned], axis=0)
        upper_first = jnp.concatenate([returned, mine], axis=0)
        return carry, jnp.where(upper == 0, lower_first, upper_first)

    crosses = lax.scan(one_round, 0, round_masks)[1]
    return (crosses, auto_spectra)


def solution(mesh):
    placed = (P("chan", "freq"), P(), P())
    return jax.shard_map(
        body,
        mesh=mesh,
        in_specs=placed,
        out_specs=(P(None, "freq", None, "chan", None), P("freq", None, "chan", None)),
        check_vma=False,
    )
```
